512 devices in a mesh: dp: 16 (over y, core), expert: 32 (over x, z).
Axes of the slice: x: 4, y: 8, z: 8, core: 2. Of those that a mesh axis runs over, the one named last changes fastest.
Arguments:
- tokens: bfloat16 [65536, 1024], P(('dp', 'expert')), may hold values from -6 to 6
- routes: int32 [65536, 4], P(('dp', 'expert')), may hold values from 0 to 31, all different within a row; in each aligned block of 128 rows (0 to 127, 128 to 255, ...) at most 32 rows name the same one
- gates: float32 [65536, 4], P(('dp', 'expert')), may hold values from 0.05 to 0.5
- w_in: bfloat16 [32, 1024, 768], P('expert', 'dp'), may hold values from -6 to 6
- w_down: bfloat16 [32, 384, 1024], P('expert', 'dp'), may hold values from -6 to 6
- out_grad: bfloat16 [65536, 1024], P(('dp', 'expert')), may hold values from -6 to 6
Outputs:
- moe_out: bfloat16 [65536, 1024], P(('dp', 'expert'))
- token_grad: bfloat16 [65536, 1024], P(('dp', 'expert'))
- new_w_in: bfloat16 [32, 1024, 768], P('expert', 'dp')
- new_w_down: bfloat16 [32, 384, 1024], P('expert', 'dp')
The draws below stay inside these ranges and needn't reach their ends.
Inputs may be any that keep to these rules, and one draw needn't show every extreme that they name: `routes`: within one device's 128 tokens no expert is named more than 32 times, a bound that some block reaches; a token names 4 different experts.
All inputs are finite; a program needn't handle non-finite values.
Results may differ from the reference program's by a relative error of at most 0.014.
Values may be sent and summed in bfloat16 or wider, within the bound.
No kernel may reach another device: no remote copies, remote signals or barrier semaphores. Data moves between devices by JAX's collectives and lax.ppermute only.
A program may use at most 64 MiB of HBM per device.

```python
import math
from functools import partial
import jax
import jax.numpy as jnp
import numpy as np
from jax import lax

D = 1024
F = 384
TOPK = 4
TOK_DEV = 128
EXPERTS = 32
CAP = 32
TOKENS = 65536
N_DP = 16
N_EXPERT = 32


def shard_levels(rng, shape, split, smallest, largest):
    def one(dim, shards_of):
        draws = jax.random.uniform(jax.random.fold_in(jax.random.fold_in(rng, 6), dim), (shards_of,), jnp.float32, smallest / len(split), largest / len(split))
        return jnp.repeat(jnp.exp(draws), shape[dim] // shards_of).reshape((-1,) + (1,) * (len(shape) - dim - 1))

    loudness = one(*split[0])
    for cut in split[1:]:
        loudness = loudness * one(*cut)
    return loudness


def deal_out(rng, own, number, rows, count, top, bound, skew):
    ranking = jax.random.permutation(rng, count)
    crowded, ordinary = load_shares(count, rows * top, bound, skew, True), load_shares(count, rows * top, bound, skew, False)
    places = jnp.arange(count)

    def named(lengths, turn):
        used = int((lengths > 0).sum())
        fixed = max(1, used // 4)
        shifted = fixed + (places - fixed + turn * (used - fixed)) % max(1, count - fixed)
        return jnp.zeros((count,), jnp.int32).at[ranking[jnp.where(places < fixed, places, shifted)]].set(jnp.asarray(lengths, jnp.int32))

    lengths = jnp.where(number % 4 == 0, named(crowded, number // 4), named(ordinary, number - number // 4 - 1))
    mixed = jax.random.permutation(jax.random.fold_in(own, 3), count)
    giver, sink = mixed[0:count // 2 * 2:2], mixed[1:count // 2 * 2:2]
    margin = jnp.minimum(lengths[giver] - 1, bound - lengths[sink]) // 2
    margin = jnp.where((giver == ranking[0]) | (sink == ranking[0]) | (lengths[sink] == 0), 0, jnp.maximum(margin, 0))
    shifted = jax.random.randint(jax.random.fold_in(own, 4), (count // 2,), 0, 1 << 20) % (margin + 1)
    lengths = lengths.at[giver].add(-shifted).at[sink].add(shifted)
    items = jnp.searchsorted(jnp.cumsum(lengths), jnp.arange(rows * top), side="right").astype(jnp.int32)
    listing = items.reshape(top, rows).T
    listing = listing[jax.random.permutation(jax.random.fold_in(own, 1), rows)]
    turn = jax.random.randint(jax.random.fold_in(own, 2), (rows, 1), 0, top)
    return jnp.take_along_axis(listing, (jnp.arange(top)[None, :] + turn) % top, axis=1)


def load_shares(amount, total, most, slope, full):
    weights = [(1 << 20) // math.isqrt(rank ** slope) + 1 for rank in range(1, amount + 1)]
    largest = most if full else min(most, max(-(-total // amount), total * weights[0] // sum(weights)))
    least = 1 if total - largest >= amount - 1 else 0
    holding, spare = [largest] + [least] * (amount - 1), total - largest - least * (amount - 1)
    while spare > 0:
        free = [i for i in range(1, amount) if holding[i] < largest] or [i for i in range(1, amount) if holding[i] < most]
        mass, left = sum([weights[i] for i in free]), spare
        for i in free:
            extra = min(most - holding[i], max(1, left * weights[i] // mass), spare)
            holding[i] = holding[i] + extra
            spare = spare - extra
    return np.array(holding)


def centred(rng, shape, spread, limit, cuts=(), kind=jnp.bfloat16):
    values = jax.random.normal(rng, shape, jnp.float32) * spread
    if len(cuts) > 0:
        values = shard_levels(rng, shape, cuts, -0.22, 0.18) * values
    return jnp.clip(values, min=-limit, max=limit).astype(kind)


def setup_inputs(seed: int = 0) -> dict:
    keys = jax.random.split(jax.random.key(seed), 7)
    tokens = centred(keys[0], (TOKENS, D), 1.0, 6.0, ((0, 512),))
    routes_keys = jax.random.split(jax.random.fold_in(keys[1], 1), TOKENS // TOK_DEV)
    routes_turns = jax.random.permutation(jax.random.fold_in(keys[1], 3), TOKENS // TOK_DEV)
    routes = jax.vmap(lambda own, number: deal_out(jax.random.fold_in(keys[1], 2), own, number, TOK_DEV, EXPERTS, TOPK, CAP, 2))(routes_keys, routes_turns).reshape((TOKENS, TOPK))
    gates = jnp.clip(jnp.exp(math.log(0.5) - 2.3025851 * jax.random.uniform(keys[2], (TOKENS, TOPK), jnp.float32) ** shard_levels(keys[2], (TOKENS, TOPK), ((0, 512),), -0.2, 0.2)), 0.05, 0.5)
    w_in = centred(keys[3], (EXPERTS, D, 2 * F), 1.0, 6.0, ((0, 32), (1, 16)))
    w_down = centred(keys[4], (EXPERTS, F, D), 1.0, 6.0, ((0, 32), (1, 16)))
    out_grad = centred(keys[5], (TOKENS, D), 1.0, 6.0, ((0, 512),))
    return {"tokens": tokens, "routes": routes, "gates": gates, "w_in": w_in, "w_down": w_down, "out_grad": out_grad}


step_rate = 0.5


def slot_numbers(route_rows, experts, capacity):
    flat_routes = route_rows.reshape(-1)
    one_hot = (flat_routes[:, None] == jnp.arange(experts, dtype=jnp.int32)[None, :]).astype(jnp.int32)
    running = jnp.cumsum(one_hot, axis=0)
    position = jnp.sum(one_hot * running, axis=1) - 1
    return (flat_routes * capacity + position).astype(jnp.int32)


def place_rows(rows, slot_index, total):
    return jnp.zeros((total, rows.shape[-1]), rows.dtype).at[slot_index].set(rows)


def pick_rows(rows, slot_index):
    return rows[slot_index]


def reference(tokens, routes, gates, w_in, w_down, out_grad):
    experts = EXPERTS
    capacity = CAP
    rows_in = TOK_DEV * TOPK
    token_of = jnp.arange(rows_in, dtype=jnp.int32) // TOPK
    scale_in = D ** -0.5
    scale_down = F ** -0.5
    total = experts * capacity

    def to_experts(sent):
        return sent.reshape(N_EXPERT, experts, capacity, D).transpose(1, 0, 2, 3).reshape(experts, N_EXPERT * capacity, D)

    def to_sources(done):
        return done.reshape(experts, N_EXPERT, capacity, D).transpose(1, 0, 2, 3).reshape(N_EXPERT, total, D)

    def group_step(totals, group_items):
        tok_group, route_group, gate_group, grad_group = group_items
        slot_index = jax.vmap(partial(slot_numbers, experts=experts, capacity=capacity))(route_group)
        placer = jax.vmap(partial(place_rows, total=total))
        send_inputs = placer(tok_group[:, token_of], slot_index)
        scaled = (gate_group.reshape(N_EXPERT, rows_in, 1) * grad_group[:, token_of].astype(jnp.float32)).astype(jnp.bfloat16)
        send_grads = placer(scaled, slot_index)
        inputs = to_experts(send_inputs)
        grad_rows = to_experts(send_grads)
        projected = jnp.einsum("erd,edj->erj", inputs.astype(jnp.float32), w_in.astype(jnp.float32)) * scale_in
        gate_part = projected[..., :F]
        up_part = projected[..., F:]
        activation = (jax.nn.silu(gate_part) * up_part).astype(jnp.bfloat16)
        results = (jnp.einsum("erf,efd->erd", activation.astype(jnp.float32), w_down.astype(jnp.float32)) * scale_down).astype(jnp.bfloat16)
        grad_act = jnp.einsum("erd,efd->erf", grad_rows.astype(jnp.float32), w_down.astype(jnp.float32)) * scale_down
        sigmoid_gate = jax.nn.sigmoid(gate_part)
        grad_gate = grad_act * up_part * sigmoid_gate * (1.0 + gate_part * (1.0 - sigmoid_gate))
        grad_up = grad_act * jax.nn.silu(gate_part)
        grad_hidden = jnp.concatenate([grad_gate, grad_up], axis=-1).astype(jnp.bfloat16)
        grad_inputs = (jnp.einsum("erj,edj->erd", grad_hidden.astype(jnp.float32), w_in.astype(jnp.float32)) * scale_in).astype(jnp.bfloat16)
        grad_in = (jnp.einsum("erd,erj->edj", inputs.astype(jnp.float32), grad_hidden.astype(jnp.float32)) * scale_in).astype(jnp.bfloat16)
        grad_down = (jnp.einsum("erf,erd->efd", activation.astype(jnp.float32), grad_rows.astype(jnp.float32)) * scale_down).astype(jnp.bfloat16)
        picked = jax.vmap(pick_rows)(to_sources(results), slot_index).astype(jnp.float32)
        picked = picked.reshape(N_EXPERT, TOK_DEV, TOPK, D)
        moe_group = jnp.sum(picked * gate_group[..., None], axis=2).astype(jnp.bfloat16)
        back_rows = jax.vmap(pick_rows)(to_sources(grad_inputs), slot_index).astype(jnp.float32)
        token_group = jnp.sum(back_rows.reshape(N_EXPERT, TOK_DEV, TOPK, D), axis=2).astype(jnp.bfloat16)
        new_totals = (totals[0] + grad_in.astype(jnp.float32), totals[1] + grad_down.astype(jnp.float32))
        return new_totals, (moe_group, token_group)

    group_items = (tokens.reshape(N_DP, N_EXPERT, TOK_DEV, D),
                   routes.reshape(N_DP, N_EXPERT, TOK_DEV, TOPK),
                   gates.reshape(N_DP, N_EXPERT, TOK_DEV, TOPK),
                   out_grad.reshape(N_DP, N_EXPERT, TOK_DEV, D))
    start_totals = (jnp.zeros(w_in.shape, jnp.float32), jnp.zeros(w_down.shape, jnp.float32))
    totals, outputs = lax.scan(group_step, start_totals, group_items)
    moe_out = outputs[0].reshape(TOKENS, D)
    token_grad = outputs[1].reshape(TOKENS, D)
    new_w_in = (w_in.astype(jnp.float32) - step_rate * totals[0]).astype(jnp.bfloat16)
    new_w_down = (w_down.astype(jnp.float32) - step_rate * totals[1]).astype(jnp.bfloat16)
    return (moe_out, token_grad, new_w_in, new_w_down)
```

```python
import jax
import jax.numpy as jnp
from jax import lax
from jax.sharding import PartitionSpec as P

step_rate = 0.5


def slot_numbers(route_rows, experts, capacity):
    flat_routes = route_rows.reshape(-1)
    one_hot = (flat_routes[:, None] == jnp.arange(experts, dtype=jnp.int32)[None, :]).astype(
        jnp.int32
    )
    running = jnp.cumsum(one_hot, axis=0)
    position = jnp.sum(one_hot * running, axis=1) - 1
    return flat_routes * capacity + position


def expert_forward(inputs, full_in, full_down):
    model_width = full_in.shape[1]
    hidden_units = full_down.shape[1]
    projected = jnp.einsum(
        "sxcd,xdj->sxcj", inputs, full_in, preferred_element_type=jnp.float32
    ) * model_width ** (-0.5)
    gate_part = projected[..., :hidden_units]
    up_part = projected[..., hidden_units:]
    activation = (jax.nn.silu(gate_part) * up_part).astype(jnp.bfloat16)
    results = (
        jnp.einsum("sxcf,xfd->sxcd", activation, full_down, preferred_element_type=jnp.float32)
        * hidden_units ** (-0.5)
    ).astype(jnp.bfloat16)
    return (projected, activation, results)


def expert_backward(projected, grad_rows, full_in, full_down):
    model_width = full_in.shape[1]
    hidden_units = full_down.shape[1]
    grad_act = jnp.einsum(
        "sxcd,xfd->sxcf", grad_rows, full_down, preferred_element_type=jnp.float32
    ) * hidden_units ** (-0.5)
    gate_part = projected[..., :hidden_units]
    up_part = projected[..., hidden_units:]
    sigmoid_gate = jax.nn.sigmoid(gate_part)
    grad_gate = grad_act * up_part * sigmoid_gate * (1.0 + gate_part * (1.0 - sigmoid_gate))
    grad_up = grad_act * jax.nn.silu(gate_part)
    grad_hidden = jnp.concatenate([grad_gate, grad_up], axis=-1).astype(jnp.bfloat16)
    grad_inputs = (
        jnp.einsum("sxcj,xdj->sxcd", grad_hidden, full_in, preferred_element_type=jnp.float32)
        * model_width ** (-0.5)
    ).astype(jnp.bfloat16)
    return (grad_hidden, grad_inputs)


def to_owner_rows(grad, owners):
    per_device, rows, cols = grad.shape
    part = rows // owners
    return (
        grad.reshape(per_device, owners, part, cols)
        .transpose(1, 0, 2, 3)
        .reshape(owners, per_device * part * cols)
    )


def from_owner_rows(flat, owners, per_device, part, cols):
    return (
        flat.reshape(owners, per_device, part, cols)
        .transpose(1, 0, 2, 3)
        .reshape(per_device, owners * part, cols)
    )


def body(tokens, routes, gates, w_in, w_down, out_grad):
    tok_rows, model_width = tokens.shape
    top_count = routes.shape[1]
    per_device, in_rows, in_cols = w_in.shape
    _, down_rows, down_cols = w_down.shape
    hidden_units = in_cols // 2
    sources = lax.axis_size("expert")
    owners = lax.axis_size("dp")
    experts = per_device * sources
    capacity = min(tok_rows, 2 * tok_rows * top_count // experts)
    total = experts * capacity

    in_size = in_rows * in_cols
    packed_w = jnp.concatenate(
        [w_in.reshape(1, per_device * in_size), w_down.reshape(1, per_device * down_rows * down_cols)],
        axis=1,
    )
    gathered = lax.all_gather(packed_w, "dp", axis=0, tiled=True)
    full_in = from_owner_rows(gathered[:, : per_device * in_size], owners, per_device, in_rows, in_cols)
    full_down = from_owner_rows(
        gathered[:, per_device * in_size :], owners, per_device, down_rows, down_cols
    )

    slot_index = slot_numbers(routes, experts, capacity).reshape(tok_rows, top_count)
    match = slot_index[None, :, :] == jnp.arange(total, dtype=jnp.int32)[:, None, None]
    pick = jnp.any(match, axis=2).astype(jnp.bfloat16)
    gate_of_slot = jnp.sum(jnp.where(match, gates[None, :, :], 0.0), axis=(1, 2))
    layout = (sources, per_device, capacity, model_width)
    send_inputs = jnp.dot(pick, tokens, preferred_element_type=jnp.float32).astype(jnp.bfloat16)
    grad_of_slot = jnp.dot(pick, out_grad, preferred_element_type=jnp.float32)
    send_grads = (gate_of_slot[:, None] * grad_of_slot).astype(jnp.bfloat16)

    inputs_here = lax.all_to_all(
        send_inputs.reshape(layout), "expert", split_axis=0, concat_axis=0, tiled=True
    )
    grad_rows = lax.all_to_all(
        send_grads.reshape(layout), "expert", split_axis=0, concat_axis=0, tiled=True
    )
    projected_here, activation_here, results_here = expert_forward(inputs_here, full_in, full_down)
    results_home = lax.all_to_all(results_here, "expert", split_axis=0, concat_axis=0, tiled=True)
    grad_hidden, grad_inputs = expert_backward(projected_here, grad_rows, full_in, full_down)

    grad_in = (
        jnp.einsum("sxcd,sxcj->xdj", inputs_here, grad_hidden, preferred_element_type=jnp.float32)
        * model_width ** (-0.5)
    ).astype(jnp.bfloat16)
    grad_down = (
        jnp.einsum("sxcf,sxcd->xfd", activation_here, grad_rows, preferred_element_type=jnp.float32)
        * hidden_units ** (-0.5)
    ).astype(jnp.bfloat16)
    packed_g = jnp.concatenate([to_owner_rows(grad_in, owners), to_owner_rows(grad_down, owners)], axis=1)
    packed_g = packed_g.reshape(owners * 8, -1)
    summed = lax.psum_scatter(packed_g, "dp", scatter_dimension=0, tiled=True)
    summed = summed.reshape(1, -1).astype(jnp.float32)
    summed_in = from_owner_rows(summed[:, : per_device * in_size], 1, per_device, in_rows, in_cols)
    summed_down = from_owner_rows(
        summed[:, per_device * in_size :], 1, per_device, down_rows, down_cols
    )

    inputs_back = lax.all_to_all(grad_inputs, "expert", split_axis=0, concat_axis=0, tiled=True)

    combine = jnp.sum(jnp.where(match, gates[None, :, :], 0.0), axis=2)
    moe_out = jnp.einsum(
        "st,sd->td",
        combine,
        results_home.reshape(total, model_width).astype(jnp.float32),
        precision=lax.Precision.HIGHEST,
        preferred_element_type=jnp.float32,
    ).astype(jnp.bfloat16)
    token_grad = jnp.einsum(
        "st,sd->td",
        pick,
        inputs_back.reshape(total, model_width),
        preferred_element_type=jnp.float32,
    ).astype(jnp.bfloat16)

    new_w_in = (w_in.astype(jnp.float32) - step_rate * summed_in).astype(jnp.bfloat16)
    new_w_down = (w_down.astype(jnp.float32) - step_rate * summed_down).astype(jnp.bfloat16)
    return (moe_out, token_grad, new_w_in, new_w_down)


def solution(mesh):
    return jax.shard_map(
        body,
        mesh=mesh,
        in_specs=(
            P(("dp", "expert"), None),
            P(("dp", "expert"), None),
            P(("dp", "expert"), None),
            P("expert", "dp", None),
            P("expert", "dp", None),
            P(("dp", "expert"), None),
        ),
        out_specs=(
            P(("dp", "expert"), None),
            P(("dp", "expert"), None),
            P("expert", "dp", None),
            P("expert", "dp", None),
        ),
        check_vma=False,
    )
```

```python
import jax
import jax.numpy as jnp
from jax import lax
from jax.sharding import PartitionSpec as P

step_rate = 0.5


def slot_numbers(route_rows, experts, capacity):
    flat_routes = route_rows.reshape(-1)
    one_hot = (flat_routes[:, None] == jnp.arange(experts, dtype=jnp.int32)[None, :]).astype(
        jnp.int32
    )
    running = jnp.cumsum(one_hot, axis=0)
    position = jnp.sum(one_hot * running, axis=1) - 1
    return flat_routes * capacity + position


def expert_forward(inputs, full_in, full_down):
    model_width = full_in.shape[1]
    hidden_units = full_down.shape[1]
    projected = jnp.einsum(
        "sxcd,xdj->sxcj", inputs, full_in, preferred_element_type=jnp.float32
    ) * model_width ** (-0.5)
    gate_part = projected[..., :hidden_units]
    up_part = projected[..., hidden_units:]
    activation = (jax.nn.silu(gate_part) * up_part).astype(jnp.bfloat16)
    results = (
        jnp.einsum("sxcf,xfd->sxcd", activation, full_down, preferred_element_type=jnp.float32)
        * hidden_units ** (-0.5)
    ).astype(jnp.bfloat16)
    return (projected, activation, results)


def expert_backward(projected, grad_rows, full_in, full_down):
    model_width = full_in.shape[1]
    hidden_units = full_down.shape[1]
    grad_act = jnp.einsum(
        "sxcd,xfd->sxcf", grad_rows, full_down, preferred_element_type=jnp.float32
    ) * hidden_units ** (-0.5)
    gate_part = projected[..., :hidden_units]
    up_part = projected[..., hidden_units:]
    sigmoid_gate = jax.nn.sigmoid(gate_part)
    grad_gate = grad_act * up_part * sigmoid_gate * (1.0 + gate_part * (1.0 - sigmoid_gate))
    grad_up = grad_act * jax.nn.silu(gate_part)
    grad_hidden = jnp.concatenate([grad_gate, grad_up], axis=-1).astype(jnp.bfloat16)
    grad_inputs = (
        jnp.einsum("sxcj,xdj->sxcd", grad_hidden, full_in, preferred_element_type=jnp.float32)
        * model_width ** (-0.5)
    ).astype(jnp.bfloat16)
    return (grad_hidden, grad_inputs)


def to_owner_rows(grad, owners):
    per_device, rows, cols = grad.shape
    part = rows // owners
    return (
        grad.reshape(per_device, owners, part, cols)
        .transpose(1, 0, 2, 3)
        .reshape(owners, per_device * part * cols)
    )


def from_owner_rows(flat, owners, per_device, part, cols):
    return (
        flat.reshape(owners, per_device, part, cols)
        .transpose(1, 0, 2, 3)
        .reshape(per_device, owners * part, cols)
    )


def body(tokens, routes, gates, w_in, w_down, out_grad):
    tok_rows, model_width = tokens.shape
    top_count = routes.shape[1]
    per_device, in_rows, in_cols = w_in.shape
    _, down_rows, down_cols = w_down.shape
    hidden_units = in_cols // 2
    sources = lax.axis_size("expert")
    owners = lax.axis_size("dp")
    experts = per_device * sources
    capacity = min(tok_rows, 2 * tok_rows * top_count // experts)
    total = experts * capacity

    in_size = in_rows * in_cols
    packed_w = jnp.concatenate(
        [w_in.reshape(1, per_device * in_size), w_down.reshape(1, per_device * down_rows * down_cols)],
        axis=1,
    )
    gathered = lax.all_gather(packed_w, "dp", axis=0, tiled=True)
    full_in = from_owner_rows(gathered[:, : per_device * in_size], owners, per_device, in_rows, in_cols)
    full_down = from_owner_rows(
        gathered[:, per_device * in_size :], owners, per_device, down_rows, down_cols
    )

    slot_index = slot_numbers(routes, experts, capacity).reshape(tok_rows, top_count)
    match = slot_index[None, :, :] == jnp.arange(total, dtype=jnp.int32)[:, None, None]
    pick = jnp.any(match, axis=2).astype(jnp.bfloat16)
    gate_of_slot = jnp.sum(jnp.where(match, gates[None, :, :], 0.0), axis=(1, 2))
    layout = (sources, per_device, capacity, model_width)
    send_inputs = jnp.dot(pick, tokens, preferred_element_type=jnp.float32).astype(jnp.bfloat16)
    grad_of_slot = jnp.dot(pick, out_grad, preferred_element_type=jnp.float32)
    send_grads = (gate_of_slot[:, None] * grad_of_slot).astype(jnp.bfloat16)

    inputs_here = lax.all_to_all(
        send_inputs.reshape(layout), "expert", split_axis=0, concat_axis=0, tiled=True
    )
    grad_rows = lax.all_to_all(
        send_grads.reshape(layout), "expert", split_axis=0, concat_axis=0, tiled=True
    )
    projected_here, activation_here, results_here = lax.optimization_barrier(
        expert_forward(inputs_here, full_in, full_down)
    )
    results_home = lax.all_to_all(results_here, "expert", split_axis=0, concat_axis=0, tiled=True)
    grad_hidden, grad_inputs = expert_backward(projected_here, grad_rows, full_in, full_down)

    grad_in = (
        jnp.einsum("sxcd,sxcj->xdj", inputs_here, grad_hidden, preferred_element_type=jnp.float32)
        * model_width ** (-0.5)
    ).astype(jnp.bfloat16)
    grad_down = (
        jnp.einsum("sxcf,sxcd->xfd", activation_here, grad_rows, preferred_element_type=jnp.float32)
        * hidden_units ** (-0.5)
    ).astype(jnp.bfloat16)
    packed_g = jnp.concatenate([to_owner_rows(grad_in, owners), to_owner_rows(grad_down, owners)], axis=1)
    packed_g = packed_g.reshape(owners * 8, -1)
    summed = lax.psum_scatter(packed_g, "dp", scatter_dimension=0, tiled=True)
    summed = summed.reshape(1, -1).astype(jnp.float32)
    summed_in = from_owner_rows(summed[:, : per_device * in_size], 1, per_device, in_rows, in_cols)
    summed_down = from_owner_rows(
        summed[:, per_device * in_size :], 1, per_device, down_rows, down_cols
    )

    inputs_back = lax.all_to_all(grad_inputs, "expert", split_axis=0, concat_axis=0, tiled=True)

    combine = jnp.sum(jnp.where(match, gates[None, :, :], 0.0), axis=2)
    moe_out = jnp.einsum(
        "st,sd->td",
        combine,
        results_home.reshape(total, model_width).astype(jnp.float32),
        precision=lax.Precision.HIGHEST,
        preferred_element_type=jnp.float32,
    ).astype(jnp.bfloat16)
    token_grad = jnp.einsum(
        "st,sd->td",
        pick,
        inputs_back.reshape(total, model_width),
        preferred_element_type=jnp.float32,
    ).astype(jnp.bfloat16)

    new_w_in = (w_in.astype(jnp.float32) - step_rate * summed_in).astype(jnp.bfloat16)
    new_w_down = (w_down.astype(jnp.float32) - step_rate * summed_down).astype(jnp.bfloat16)
    return (moe_out, token_grad, new_w_in, new_w_down)


def solution(mesh):
    return jax.shard_map(
        body,
        mesh=mesh,
        in_specs=(
            P(("dp", "expert"), None),
            P(("dp", "expert"), None),
            P(("dp", "expert"), None),
            P("expert", "dp", None),
            P("expert", "dp", None),
            P(("dp", "expert"), None),
        ),
        out_specs=(
            P(("dp", "expert"), None),
            P(("dp", "expert"), None),
            P("expert", "dp", None),
            P("expert", "dp", None),
        ),
        check_vma=False,
    )
```

```python
import jax
import jax.numpy as jnp
from jax import lax
from jax.sharding import PartitionSpec as P

step_rate = 0.5


def slot_numbers(route_rows, experts, capacity):
    flat_routes = route_rows.reshape(-1)
    one_hot = (flat_routes[:, None] == jnp.arange(experts, dtype=jnp.int32)[None, :]).astype(
        jnp.int32
    )
    running = jnp.cumsum(one_hot, axis=0)
    position = jnp.sum(one_hot * running, axis=1) - 1
    return flat_routes * capacity + position


def expert_forward(inputs, full_in, full_down):
    model_width = full_in.shape[1]
    hidden_units = full_down.shape[1]
    projected = jnp.einsum(
        "sxcd,xdj->sxcj", inputs, full_in, preferred_element_type=jnp.float32
    ) * model_width ** (-0.5)
    gate_part = projected[..., :hidden_units]
    up_part = projected[..., hidden_units:]
    activation = (jax.nn.silu(gate_part) * up_part).astype(jnp.bfloat16)
    results = (
        jnp.einsum("sxcf,xfd->sxcd", activation, full_down, preferred_element_type=jnp.float32)
        * hidden_units ** (-0.5)
    ).astype(jnp.bfloat16)
    return (projected, activation, results)


def expert_backward(projected, grad_rows, full_in, full_down):
    model_width = full_in.shape[1]
    hidden_units = full_down.shape[1]
    grad_act = jnp.einsum(
        "sxcd,xfd->sxcf", grad_rows, full_down, preferred_element_type=jnp.float32
    ) * hidden_units ** (-0.5)
    gate_part = projected[..., :hidden_units]
    up_part = projected[..., hidden_units:]
    sigmoid_gate = jax.nn.sigmoid(gate_part)
    grad_gate = grad_act * up_part * sigmoid_gate * (1.0 + gate_part * (1.0 - sigmoid_gate))
    grad_up = grad_act * jax.nn.silu(gate_part)
    grad_hidden = jnp.concatenate([grad_gate, grad_up], axis=-1).astype(jnp.bfloat16)
    grad_inputs = (
        jnp.einsum("sxcj,xdj->sxcd", grad_hidden, full_in, preferred_element_type=jnp.float32)
        * model_width ** (-0.5)
    ).astype(jnp.bfloat16)
    return (grad_hidden, grad_inputs)


def to_owner_rows(grad, owners):
    per_device, rows, cols = grad.shape
    part = rows // owners
    return (
        grad.reshape(per_device, owners, part, cols)
        .transpose(1, 0, 2, 3)
        .reshape(owners, per_device * part * cols)
    )


def from_owner_rows(flat, owners, per_device, part, cols):
    return (
        flat.reshape(owners, per_device, part, cols)
        .transpose(1, 0, 2, 3)
        .reshape(per_device, owners * part, cols)
    )


def body(tokens, routes, gates, w_in, w_down, out_grad):
    tok_rows, model_width = tokens.shape
    top_count = routes.shape[1]
    per_device, in_rows, in_cols = w_in.shape
    _, down_rows, down_cols = w_down.shape
    hidden_units = in_cols // 2
    sources = lax.axis_size("expert")
    owners = lax.axis_size("dp")
    experts = per_device * sources
    capacity = min(tok_rows, 2 * tok_rows * top_count // experts)
    total = experts * capacity

    in_size = in_rows * in_cols
    packed_w = jnp.concatenate(
        [w_in.reshape(1, per_device * in_size), w_down.reshape(1, per_device * down_rows * down_cols)],
        axis=1,
    )
    gathered = lax.all_gather(packed_w, "dp", axis=0, tiled=True)
    full_in = from_owner_rows(gathered[:, : per_device * in_size], owners, per_device, in_rows, in_cols)
    full_down = from_owner_rows(
        gathered[:, per_device * in_size :], owners, per_device, down_rows, down_cols
    )

    slot_index = slot_numbers(routes, experts, capacity).reshape(tok_rows, top_count)
    match = slot_index[None, :, :] == jnp.arange(total, dtype=jnp.int32)[:, None, None]
    pick = jnp.any(match, axis=2).astype(jnp.bfloat16)
    gate_of_slot = jnp.sum(jnp.where(match, gates[None, :, :], 0.0), axis=(1, 2))
    layout = (sources, per_device, capacity, model_width)
    send_inputs = jnp.dot(pick, tokens, preferred_element_type=jnp.float32).astype(jnp.bfloat16)
    grad_of_slot = jnp.dot(pick, out_grad, preferred_element_type=jnp.float32)
    send_grads = (gate_of_slot[:, None] * grad_of_slot).astype(jnp.bfloat16)

    inputs_here = lax.all_to_all(
        send_inputs.reshape(layout), "expert", split_axis=0, concat_axis=0, tiled=True
    )
    grad_rows = lax.all_to_all(
        send_grads.reshape(layout), "expert", split_axis=0, concat_axis=0, tiled=True
    )
    projected_here, activation_here, results_here = lax.optimization_barrier(
        expert_forward(inputs_here, full_in, full_down)
    )
    results_home = lax.all_to_all(results_here, "expert", split_axis=0, concat_axis=0, tiled=True)
    grad_hidden, grad_inputs = expert_backward(projected_here, grad_rows, full_in, full_down)

    grad_in = (
        jnp.einsum("sxcd,sxcj->xdj", inputs_here, grad_hidden, preferred_element_type=jnp.float32)
        * model_width ** (-0.5)
    ).astype(jnp.bfloat16)
    grad_down = (
        jnp.einsum("sxcf,sxcd->xfd", activation_here, grad_rows, preferred_element_type=jnp.float32)
        * hidden_units ** (-0.5)
    ).astype(jnp.bfloat16)
    packed_g = jnp.concatenate([to_owner_rows(grad_in, owners), to_owner_rows(grad_down, owners)], axis=1)
    packed_g = packed_g.reshape(owners * 8, -1)
    summed = lax.psum_scatter(packed_g, "dp", scatter_dimension=0, tiled=True)
    summed = summed.reshape(1, -1).astype(jnp.float32)
    summed_in = from_owner_rows(summed[:, : per_device * in_size], 1, per_device, in_rows, in_cols)
    summed_down = from_owner_rows(
        summed[:, per_device * in_size :], 1, per_device, down_rows, down_cols
    )

    inputs_back = lax.all_to_all(grad_inputs, "expert", split_axis=0, concat_axis=0, tiled=True)

    new_w_in = (w_in.astype(jnp.float32) - step_rate * summed_in).astype(jnp.bfloat16)
    new_w_down = (w_down.astype(jnp.float32) - step_rate * summed_down).astype(jnp.bfloat16)
    inputs_back, new_w_in, new_w_down = lax.optimization_barrier((inputs_back, new_w_in, new_w_down))

    combine = jnp.sum(jnp.where(match, gates[None, :, :], 0.0), axis=2)
    moe_out = jnp.einsum(
        "st,sd->td",
        combine,
        results_home.reshape(total, model_width).astype(jnp.float32),
        precision=lax.Precision.HIGHEST,
        preferred_element_type=jnp.float32,
    ).astype(jnp.bfloat16)
    token_grad = jnp.einsum(
        "st,sd->td",
        pick,
        inputs_back.reshape(total, model_width),
        preferred_element_type=jnp.float32,
    ).astype(jnp.bfloat16)

    return (moe_out, token_grad, new_w_in, new_w_down)


def solution(mesh):
    return jax.shard_map(
        body,
        mesh=mesh,
        in_specs=(
            P(("dp", "expert"), None),
            P(("dp", "expert"), None),
            P(("dp", "expert"), None),
            P("expert", "dp", None),
            P("expert", "dp", None),
            P(("dp", "expert"), None),
        ),
        out_specs=(
            P(("dp", "expert"), None),
            P(("dp", "expert"), None),
            P("expert", "dp", None),
            P("expert", "dp", None),
        ),
        check_vma=False,
    )
```

```python
import jax
import jax.numpy as jnp
from jax import lax
from jax.sharding import PartitionSpec as P

step_rate = 0.5


def slot_numbers(route_rows, experts, capacity):
    flat_routes = route_rows.reshape(-1)
    one_hot = (flat_routes[:, None] == jnp.arange(experts, dtype=jnp.int32)[None, :]).astype(
        jnp.int32
    )
    running = jnp.cumsum(one_hot, axis=0)
    position = jnp.sum(one_hot * running, axis=1) - 1
    return flat_routes * capacity + position


def expert_forward(inputs, full_in, full_down):
    model_width = full_in.shape[1]
    hidden_units = full_down.shape[1]
    projected = jnp.einsum(
        "sxcd,xdj->sxcj", inputs, full_in, preferred_element_type=jnp.float32
    ) * model_width ** (-0.5)
    gate_part = projected[..., :hidden_units]
    up_part = projected[..., hidden_units:]
    activation = (jax.nn.silu(gate_part) * up_part).astype(jnp.bfloat16)
    results = (
        jnp.einsum("sxcf,xfd->sxcd", activation, full_down, preferred_element_type=jnp.float32)
        * hidden_units ** (-0.5)
    ).astype(jnp.bfloat16)
    return (projected, activation, results)


def expert_backward(projected, grad_rows, full_in, full_down):
    model_width = full_in.shape[1]
    hidden_units = full_down.shape[1]
    grad_act = jnp.einsum(
        "sxcd,xfd->sxcf", grad_rows, full_down, preferred_element_type=jnp.float32
    ) * hidden_units ** (-0.5)
    gate_part = projected[..., :hidden_units]
    up_part = projected[..., hidden_units:]
    sigmoid_gate = jax.nn.sigmoid(gate_part)
    grad_gate = grad_act * up_part * sigmoid_gate * (1.0 + gate_part * (1.0 - sigmoid_gate))
    grad_up = grad_act * jax.nn.silu(gate_part)
    grad_hidden = jnp.concatenate([grad_gate, grad_up], axis=-1).astype(jnp.bfloat16)
    grad_inputs = (
        jnp.einsum("sxcj,xdj->sxcd", grad_hidden, full_in, preferred_element_type=jnp.float32)
        * model_width ** (-0.5)
    ).astype(jnp.bfloat16)
    return (grad_hidden, grad_inputs)


def to_owner_rows(grad, owners):
    per_device, rows, cols = grad.shape
    part = rows // owners
    return (
        grad.reshape(per_device, owners, part, cols)
        .transpose(1, 0, 2, 3)
        .reshape(owners, per_device * part * cols)
    )


def from_owner_rows(flat, owners, per_device, part, cols):
    return (
        flat.reshape(owners, per_device, part, cols)
        .transpose(1, 0, 2, 3)
        .reshape(per_device, owners * part, cols)
    )


def gather_by_permutes(piece, owners):
    me = lax.axis_index("dp")
    arrived = [piece]
    for shift in range(1, owners):
        pairs = [(i, (i + shift) % owners) for i in range(owners)]
        arrived.append(lax.ppermute(piece, "dp", pairs))
    stacked = jnp.stack(arrived)
    order = (me - jnp.arange(owners, dtype=jnp.int32)) % owners
    return jnp.take(stacked, order, axis=0)


def reduce_scatter_by_permutes(parts, owners):
    me = lax.axis_index("dp")
    rotated = jnp.take(parts, (me + jnp.arange(owners, dtype=jnp.int32)) % owners, axis=0)
    total = rotated[0].astype(jnp.float32)
    for shift in range(1, owners):
        pairs = [(i, (i + shift) % owners) for i in range(owners)]
        total = total + lax.ppermute(rotated[shift], "dp", pairs).astype(jnp.float32)
    return total


def body(tokens, routes, gates, w_in, w_down, out_grad):
    tok_rows, model_width = tokens.shape
    top_count = routes.shape[1]
    per_device, in_rows, in_cols = w_in.shape
    _, down_rows, down_cols = w_down.shape
    hidden_units = in_cols // 2
    sources = lax.axis_size("expert")
    owners = lax.axis_size("dp")
    experts = per_device * sources
    capacity = min(tok_rows, 2 * tok_rows * top_count // experts)
    total = experts * capacity

    in_size = in_rows * in_cols
    packed_w = jnp.concatenate(
        [w_in.reshape(1, per_device * in_size), w_down.reshape(1, per_device * down_rows * down_cols)],
        axis=1,
    )
    gathered = gather_by_permutes(packed_w[0], owners)
    full_in = from_owner_rows(gathered[:, : per_device * in_size], owners, per_device, in_rows, in_cols)
    full_down = from_owner_rows(
        gathered[:, per_device * in_size :], owners, per_device, down_rows, down_cols
    )

    slot_index = slot_numbers(routes, experts, capacity).reshape(tok_rows, top_count)
    match = slot_index[None, :, :] == jnp.arange(total, dtype=jnp.int32)[:, None, None]
    pick = jnp.any(match, axis=2).astype(jnp.bfloat16)
    gate_of_slot = jnp.sum(jnp.where(match, gates[None, :, :], 0.0), axis=(1, 2))
    layout = (sources, per_device, capacity, model_width)
    send_inputs = jnp.dot(pick, tokens, preferred_element_type=jnp.float32).astype(jnp.bfloat16)
    grad_of_slot = jnp.dot(pick, out_grad, preferred_element_type=jnp.float32)
    send_grads = (gate_of_slot[:, None] * grad_of_slot).astype(jnp.bfloat16)

    inputs_here = lax.all_to_all(
        send_inputs.reshape(layout), "expert", split_axis=0, concat_axis=0, tiled=True
    )
    grad_rows = lax.all_to_all(
        send_grads.reshape(layout), "expert", split_axis=0, concat_axis=0, tiled=True
    )
    projected_here, activation_here, results_here = lax.optimization_barrier(
        expert_forward(inputs_here, full_in, full_down)
    )
    results_home = lax.all_to_all(results_here, "expert", split_axis=0, concat_axis=0, tiled=True)
    grad_hidden, grad_inputs = expert_backward(projected_here, grad_rows, full_in, full_down)

    grad_in = (
        jnp.einsum("sxcd,sxcj->xdj", inputs_here, grad_hidden, preferred_element_type=jnp.float32)
        * model_width ** (-0.5)
    ).astype(jnp.bfloat16)
    grad_down = (
        jnp.einsum("sxcf,sxcd->xfd", activation_here, grad_rows, preferred_element_type=jnp.float32)
        * hidden_units ** (-0.5)
    ).astype(jnp.bfloat16)
    packed_g = jnp.concatenate([to_owner_rows(grad_in, owners), to_owner_rows(grad_down, owners)], axis=1)
    summed = reduce_scatter_by_permutes(packed_g, owners).reshape(1, -1)
    summed_in = from_owner_rows(summed[:, : per_device * in_size], 1, per_device, in_rows, in_cols)
    summed_down = from_owner_rows(
        summed[:, per_device * in_size :], 1, per_device, down_rows, down_cols
    )

    inputs_back = lax.all_to_all(grad_inputs, "expert", split_axis=0, concat_axis=0, tiled=True)

    new_w_in = (w_in.astype(jnp.float32) - step_rate * summed_in).astype(jnp.bfloat16)
    new_w_down = (w_down.astype(jnp.float32) - step_rate * summed_down).astype(jnp.bfloat16)
    inputs_back, new_w_in, new_w_down = lax.optimization_barrier((inputs_back, new_w_in, new_w_down))

    combine = jnp.sum(jnp.where(match, gates[None, :, :], 0.0), axis=2)
    moe_out = jnp.einsum(
        "st,sd->td",
        combine,
        results_home.reshape(total, model_width).astype(jnp.float32),
        precision=lax.Precision.HIGHEST,
        preferred_element_type=jnp.float32,
    ).astype(jnp.bfloat16)
    token_grad = jnp.einsum(
        "st,sd->td",
        pick,
        inputs_back.reshape(total, model_width),
        preferred_element_type=jnp.float32,
    ).astype(jnp.bfloat16)

    return (moe_out, token_grad, new_w_in, new_w_down)


def solution(mesh):
    return jax.shard_map(
        body,
        mesh=mesh,
        in_specs=(
            P(("dp", "expert"), None),
            P(("dp", "expert"), None),
            P(("dp", "expert"), None),
            P("expert", "dp", None),
            P("expert", "dp", None),
            P(("dp", "expert"), None),
        ),
        out_specs=(
            P(("dp", "expert"), None),
            P(("dp", "expert"), None),
            P("expert", "dp", None),
            P("expert", "dp", None),
        ),
        check_vma=False,
    )
```

```python
import jax
import jax.numpy as jnp
from jax import lax
from jax.sharding import PartitionSpec as P

step_rate = 0.5


def expert_forward(inputs, full_in, full_down):
    model_width = full_in.shape[1]
    hidden_units = full_down.shape[1]
    projected = jnp.einsum(
        "sxcd,xdj->sxcj", inputs, full_in, preferred_element_type=jnp.float32
    ) * model_width ** (-0.5)
    gate_part = projected[..., :hidden_units]
    up_part = projected[..., hidden_units:]
    activation = (jax.nn.silu(gate_part) * up_part).astype(jnp.bfloat16)
    results = (
        jnp.einsum("sxcf,xfd->sxcd", activation, full_down, preferred_element_type=jnp.float32)
        * hidden_units ** (-0.5)
    ).astype(jnp.bfloat16)
    return (projected, activation, results)


def expert_backward(projected, grad_rows, full_in, full_down):
    model_width = full_in.shape[1]
    hidden_units = full_down.shape[1]
    grad_act = jnp.einsum(
        "sxcd,xfd->sxcf", grad_rows, full_down, preferred_element_type=jnp.float32
    ) * hidden_units ** (-0.5)
    gate_part = projected[..., :hidden_units]
    up_part = projected[..., hidden_units:]
    sigmoid_gate = jax.nn.sigmoid(gate_part)
    grad_gate = grad_act * up_part * sigmoid_gate * (1.0 + gate_part * (1.0 - sigmoid_gate))
    grad_up = grad_act * jax.nn.silu(gate_part)
    grad_hidden = jnp.concatenate([grad_gate, grad_up], axis=-1).astype(jnp.bfloat16)
    grad_inputs = (
        jnp.einsum("sxcj,xdj->sxcd", grad_hidden, full_in, preferred_element_type=jnp.float32)
        * model_width ** (-0.5)
    ).astype(jnp.bfloat16)
    return (grad_hidden, grad_inputs)


def to_owner_rows(grad, owners):
    per_device, rows, cols = grad.shape
    part = rows // owners
    return (
        grad.reshape(per_device, owners, part, cols)
        .transpose(1, 0, 2, 3)
        .reshape(owners, per_device * part * cols)
    )


def from_owner_rows(flat, owners, per_device, part, cols):
    return (
        flat.reshape(owners, per_device, part, cols)
        .transpose(1, 0, 2, 3)
        .reshape(per_device, owners * part, cols)
    )


def body(tokens, routes, gates, w_in, w_down, out_grad):
    tok_rows, model_width = tokens.shape
    top_count = routes.shape[1]
    per_device, in_rows, in_cols = w_in.shape
    _, down_rows, down_cols = w_down.shape
    hidden_units = in_cols // 2
    sources = lax.axis_size("expert")
    owners = lax.axis_size("dp")
    experts = per_device * sources
    capacity = min(tok_rows, 2 * tok_rows * top_count // experts)
    total = experts * capacity

    in_size = in_rows * in_cols
    packed_w = jnp.concatenate(
        [w_in.reshape(1, per_device * in_size), w_down.reshape(1, per_device * down_rows * down_cols)],
        axis=1,
    )
    gathered = lax.all_gather(packed_w, "dp", axis=0, tiled=True)
    full_in = from_owner_rows(gathered[:, : per_device * in_size], owners, per_device, in_rows, in_cols)
    full_down = from_owner_rows(
        gathered[:, per_device * in_size :], owners, per_device, down_rows, down_cols
    )

    named = routes[:, :, None] == jnp.arange(experts, dtype=jnp.int32)[None, None, :]
    routed = jnp.any(named, axis=1)
    gate_of = jnp.sum(jnp.where(named, gates[:, :, None], 0.0), axis=1)
    earlier = (
        jnp.arange(tok_rows, dtype=jnp.int32)[:, None] > jnp.arange(tok_rows, dtype=jnp.int32)[None, :]
    ).astype(jnp.bfloat16)
    rank = jnp.dot(earlier, routed.astype(jnp.bfloat16), preferred_element_type=jnp.float32)
    in_slot = routed.T[:, None, :] & (
        rank.T[:, None, :] == jnp.arange(capacity, dtype=jnp.float32)[None, :, None]
    )
    slot_gate = jnp.where(in_slot, gate_of.T[:, None, :], 0.0).reshape(total, tok_rows)
    pick = in_slot.reshape(total, tok_rows).astype(jnp.bfloat16)
    gate_of_slot = jnp.sum(slot_gate, axis=1)
    layout = (sources, per_device, capacity, model_width)
    send_inputs = jnp.dot(pick, tokens, preferred_element_type=jnp.float32).astype(jnp.bfloat16)
    grad_of_slot = jnp.dot(pick, out_grad, preferred_element_type=jnp.float32)
    send_grads = (gate_of_slot[:, None] * grad_of_slot).astype(jnp.bfloat16)

    inputs_here = lax.all_to_all(
        send_inputs.reshape(layout), "expert", split_axis=0, concat_axis=0, tiled=True
    )
    grad_rows = lax.all_to_all(
        send_grads.reshape(layout), "expert", split_axis=0, concat_axis=0, tiled=True
    )
    projected_here, activation_here, results_here = lax.optimization_barrier(
        expert_forward(inputs_here, full_in, full_down)
    )
    results_home = lax.all_to_all(results_here, "expert", split_axis=0, concat_axis=0, tiled=True)
    grad_hidden, grad_inputs = expert_backward(projected_here, grad_rows, full_in, full_down)

    grad_in = (
        jnp.einsum("sxcd,sxcj->xdj", inputs_here, grad_hidden, preferred_element_type=jnp.float32)
        * model_width ** (-0.5)
    ).astype(jnp.bfloat16)
    grad_down = (
        jnp.einsum("sxcf,sxcd->xfd", activation_here, grad_rows, preferred_element_type=jnp.float32)
        * hidden_units ** (-0.5)
    ).astype(jnp.bfloat16)
    packed_g = jnp.concatenate([to_owner_rows(grad_in, owners), to_owner_rows(grad_down, owners)], axis=1)
    packed_g = packed_g.reshape(owners * 8, -1)
    summed = lax.psum_scatter(packed_g, "dp", scatter_dimension=0, tiled=True)
    summed = summed.reshape(1, -1).astype(jnp.float32)
    summed_in = from_owner_rows(summed[:, : per_device * in_size], 1, per_device, in_rows, in_cols)
    summed_down = from_owner_rows(
        summed[:, per_device * in_size :], 1, per_device, down_rows, down_cols
    )

    inputs_back = lax.all_to_all(grad_inputs, "expert", split_axis=0, concat_axis=0, tiled=True)

    new_w_in = (w_in.astype(jnp.float32) - step_rate * summed_in).astype(jnp.bfloat16)
    new_w_down = (w_down.astype(jnp.float32) - step_rate * summed_down).astype(jnp.bfloat16)
    inputs_back, new_w_in, new_w_down = lax.optimization_barrier((inputs_back, new_w_in, new_w_down))

    moe_out = jnp.einsum(
        "st,sd->td",
        slot_gate,
        results_home.reshape(total, model_width).astype(jnp.float32),
        precision=lax.Precision.HIGHEST,
        preferred_element_type=jnp.float32,
    ).astype(jnp.bfloat16)
    token_grad = jnp.einsum(
        "st,sd->td",
        pick,
        inputs_back.reshape(total, model_width),
        preferred_element_type=jnp.float32,
    ).astype(jnp.bfloat16)

    return (moe_out, token_grad, new_w_in, new_w_down)


def solution(mesh):
    return jax.shard_map(
        body,
        mesh=mesh,
        in_specs=(
            P(("dp", "expert"), None),
            P(("dp", "expert"), None),
            P(("dp", "expert"), None),
            P("expert", "dp", None),
            P("expert", "dp", None),
            P(("dp", "expert"), None),
        ),
        out_specs=(
            P(("dp", "expert"), None),
            P(("dp", "expert"), None),
            P("expert", "dp", None),
            P("expert", "dp", None),
        ),
        check_vma=False,
    )
```

```python
import jax
import jax.numpy as jnp
from jax import lax
from jax.sharding import PartitionSpec as P

step_rate = 0.5


def expert_forward(inputs, full_in, full_down):
    model_width = full_in.shape[1]
    hidden_units = full_down.shape[1]
    projected = jnp.einsum(
        "sxcd,xdj->sxcj", inputs, full_in, preferred_element_type=jnp.float32
    ) * model_width ** (-0.5)
    gate_part = projected[..., :hidden_units]
    up_part = projected[..., hidden_units:]
    activation = (jax.nn.silu(gate_part) * up_part).astype(jnp.bfloat16)
    results = (
        jnp.einsum("sxcf,xfd->sxcd", activation, full_down, preferred_element_type=jnp.float32)
        * hidden_units ** (-0.5)
    ).astype(jnp.bfloat16)
    return (projected, activation, results)


def expert_backward(projected, grad_rows, full_in, full_down):
    model_width = full_in.shape[1]
    hidden_units = full_down.shape[1]
    grad_act = jnp.einsum(
        "sxcd,xfd->sxcf", grad_rows, full_down, preferred_element_type=jnp.float32
    ) * hidden_units ** (-0.5)
    gate_part = projected[..., :hidden_units]
    up_part = projected[..., hidden_units:]
    sigmoid_gate = jax.nn.sigmoid(gate_part)
    grad_gate = grad_act * up_part * sigmoid_gate * (1.0 + gate_part * (1.0 - sigmoid_gate))
    grad_up = grad_act * jax.nn.silu(gate_part)
    grad_hidden = jnp.concatenate([grad_gate, grad_up], axis=-1).astype(jnp.bfloat16)
    grad_inputs = (
        jnp.einsum("sxcj,xdj->sxcd", grad_hidden, full_in, preferred_element_type=jnp.float32)
        * model_width ** (-0.5)
    ).astype(jnp.bfloat16)
    return (grad_hidden, grad_inputs)


def to_owner_rows(grad, owners):
    per_device, rows, cols = grad.shape
    part = rows // owners
    return (
        grad.reshape(per_device, owners, part, cols)
        .transpose(1, 0, 2, 3)
        .reshape(owners, per_device * part * cols)
    )


def from_owner_rows(flat, owners, per_device, part, cols):
    return (
        flat.reshape(owners, per_device, part, cols)
        .transpose(1, 0, 2, 3)
        .reshape(per_device, owners * part, cols)
    )


def body(tokens, routes, gates, w_in, w_down, out_grad):
    tok_rows, model_width = tokens.shape
    top_count = routes.shape[1]
    per_device, in_rows, in_cols = w_in.shape
    _, down_rows, down_cols = w_down.shape
    hidden_units = in_cols // 2
    sources = lax.axis_size("expert")
    owners = lax.axis_size("dp")
    experts = per_device * sources
    capacity = min(tok_rows, 2 * tok_rows * top_count // experts)
    total = experts * capacity

    in_size = in_rows * in_cols
    packed_w = jnp.concatenate(
        [w_in.reshape(1, per_device * in_size), w_down.reshape(1, per_device * down_rows * down_cols)],
        axis=1,
    )
    gathered = lax.all_gather(packed_w, "dp", axis=0, tiled=True)
    full_in = from_owner_rows(gathered[:, : per_device * in_size], owners, per_device, in_rows, in_cols)
    full_down = from_owner_rows(
        gathered[:, per_device * in_size :], owners, per_device, down_rows, down_cols
    )

    named = routes[:, :, None] == jnp.arange(experts, dtype=jnp.int32)[None, None, :]
    routed = jnp.any(named, axis=1)
    gate_of = jnp.sum(jnp.where(named, gates[:, :, None], 0.0), axis=1)
    earlier = (
        jnp.arange(tok_rows, dtype=jnp.int32)[:, None] > jnp.arange(tok_rows, dtype=jnp.int32)[None, :]
    ).astype(jnp.bfloat16)
    rank = jnp.dot(earlier, routed.astype(jnp.bfloat16), preferred_element_type=jnp.float32)
    in_slot = routed.T[:, None, :] & (
        rank.T[:, None, :] == jnp.arange(capacity, dtype=jnp.float32)[None, :, None]
    )
    slot_gate = jnp.where(in_slot, gate_of.T[:, None, :], 0.0).reshape(total, tok_rows)
    pick = lax.optimization_barrier(in_slot.reshape(total, tok_rows).astype(jnp.bfloat16))
    gate_of_slot = jnp.sum(slot_gate, axis=1)
    layout = (sources, per_device, capacity, model_width)
    send_inputs = jnp.dot(pick, tokens, preferred_element_type=jnp.float32).astype(jnp.bfloat16)
    grad_of_slot = jnp.dot(pick, out_grad, preferred_element_type=jnp.float32)
    send_grads = (gate_of_slot[:, None] * grad_of_slot).astype(jnp.bfloat16)

    inputs_here = lax.all_to_all(
        send_inputs.reshape(layout), "expert", split_axis=0, concat_axis=0, tiled=True
    )
    grad_rows = lax.all_to_all(
        send_grads.reshape(layout), "expert", split_axis=0, concat_axis=0, tiled=True
    )
    projected_here, activation_here, results_here = lax.optimization_barrier(
        expert_forward(inputs_here, full_in, full_down)
    )
    results_home = lax.all_to_all(results_here, "expert", split_axis=0, concat_axis=0, tiled=True)
    grad_hidden, grad_inputs = expert_backward(projected_here, grad_rows, full_in, full_down)

    grad_in = (
        jnp.einsum("sxcd,sxcj->xdj", inputs_here, grad_hidden, preferred_element_type=jnp.float32)
        * model_width ** (-0.5)
    ).astype(jnp.bfloat16)
    grad_down = (
        jnp.einsum("sxcf,sxcd->xfd", activation_here, grad_rows, preferred_element_type=jnp.float32)
        * hidden_units ** (-0.5)
    ).astype(jnp.bfloat16)
    packed_g = jnp.concatenate([to_owner_rows(grad_in, owners), to_owner_rows(grad_down, owners)], axis=1)
    packed_g = packed_g.reshape(owners * 8, -1)
    summed = lax.psum_scatter(packed_g, "dp", scatter_dimension=0, tiled=True)
    summed = summed.reshape(1, -1).astype(jnp.float32)
    summed_in = from_owner_rows(summed[:, : per_device * in_size], 1, per_device, in_rows, in_cols)
    summed_down = from_owner_rows(
        summed[:, per_device * in_size :], 1, per_device, down_rows, down_cols
    )

    inputs_back = lax.all_to_all(grad_inputs, "expert", split_axis=0, concat_axis=0, tiled=True)

    new_w_in = (w_in.astype(jnp.float32) - step_rate * summed_in).astype(jnp.bfloat16)
    new_w_down = (w_down.astype(jnp.float32) - step_rate * summed_down).astype(jnp.bfloat16)
    inputs_back, new_w_in, new_w_down = lax.optimization_barrier((inputs_back, new_w_in, new_w_down))

    moe_out = jnp.einsum(
        "st,sd->td",
        slot_gate,
        results_home.reshape(total, model_width).astype(jnp.float32),
        precision=lax.Precision.HIGHEST,
        preferred_element_type=jnp.float32,
    ).astype(jnp.bfloat16)
    token_grad = jnp.einsum(
        "st,sd->td",
        pick,
        inputs_back.reshape(total, model_width),
        preferred_element_type=jnp.float32,
    ).astype(jnp.bfloat16)

    return (moe_out, token_grad, new_w_in, new_w_down)


def solution(mesh):
    return jax.shard_map(
        body,
        mesh=mesh,
        in_specs=(
            P(("dp", "expert"), None),
            P(("dp", "expert"), None),
            P(("dp", "expert"), None),
            P("expert", "dp", None),
            P("expert", "dp", None),
            P(("dp", "expert"), None),
        ),
        out_specs=(
            P(("dp", "expert"), None),
            P(("dp", "expert"), None),
            P("expert", "dp", None),
            P("expert", "dp", None),
        ),
        check_vma=False,
    )
```

```python
import jax
import jax.numpy as jnp
from jax import lax
from jax.sharding import PartitionSpec as P

step_rate = 0.5


def expert_forward(inputs, full_in, full_down):
    model_width = full_in.shape[1]
    hidden_units = full_down.shape[1]
    projected = jnp.einsum(
        "sxcd,xdj->sxcj", inputs, full_in, preferred_element_type=jnp.float32
    ) * model_width ** (-0.5)
    gate_part = projected[..., :hidden_units]
    up_part = projected[..., hidden_units:]
    activation = (jax.nn.silu(gate_part) * up_part).astype(jnp.bfloat16)
    results = (
        jnp.einsum("sxcf,xfd->sxcd", activation, full_down, preferred_element_type=jnp.float32)
        * hidden_units ** (-0.5)
    ).astype(jnp.bfloat16)
    return (projected, activation, results)


def expert_backward(projected, grad_rows, full_in, full_down):
    model_width = full_in.shape[1]
    hidden_units = full_down.shape[1]
    grad_act = jnp.einsum(
        "sxcd,xfd->sxcf", grad_rows, full_down, preferred_element_type=jnp.float32
    ) * hidden_units ** (-0.5)
    gate_part = projected[..., :hidden_units]
    up_part = projected[..., hidden_units:]
    sigmoid_gate = jax.nn.sigmoid(gate_part)
    grad_gate = grad_act * up_part * sigmoid_gate * (1.0 + gate_part * (1.0 - sigmoid_gate))
    grad_up = grad_act * jax.nn.silu(gate_part)
    grad_hidden = jnp.concatenate([grad_gate, grad_up], axis=-1).astype(jnp.bfloat16)
    grad_inputs = (
        jnp.einsum("sxcj,xdj->sxcd", grad_hidden, full_in, preferred_element_type=jnp.float32)
        * model_width ** (-0.5)
    ).astype(jnp.bfloat16)
    return (grad_hidden, grad_inputs)


def to_owner_rows(grad, owners):
    per_device, rows, cols = grad.shape
    part = rows // owners
    return (
        grad.reshape(per_device, owners, part, cols)
        .transpose(1, 0, 2, 3)
        .reshape(owners, per_device * part * cols)
    )


def from_owner_rows(flat, owners, per_device, part, cols):
    return (
        flat.reshape(owners, per_device, part, cols)
        .transpose(1, 0, 2, 3)
        .reshape(per_device, owners * part, cols)
    )


def body(tokens, routes, gates, w_in, w_down, out_grad):
    tok_rows, model_width = tokens.shape
    top_count = routes.shape[1]
    per_device, in_rows, in_cols = w_in.shape
    _, down_rows, down_cols = w_down.shape
    hidden_units = in_cols // 2
    sources = lax.axis_size("expert")
    owners = lax.axis_size("dp")
    experts = per_device * sources
    capacity = min(tok_rows, 2 * tok_rows * top_count // experts)
    total = experts * capacity

    in_size = in_rows * in_cols
    packed_w = jnp.concatenate(
        [w_in.reshape(1, per_device * in_size), w_down.reshape(1, per_device * down_rows * down_cols)],
        axis=1,
    )
    gathered = lax.all_gather(packed_w, "dp", axis=0, tiled=True)
    full_in = from_owner_rows(gathered[:, : per_device * in_size], owners, per_device, in_rows, in_cols)
    full_down = from_owner_rows(
        gathered[:, per_device * in_size :], owners, per_device, down_rows, down_cols
    )

    named = routes[:, :, None] == jnp.arange(experts, dtype=jnp.int32)[None, None, :]
    routed = jnp.any(named, axis=1)
    gate_of = jnp.sum(jnp.where(named, gates[:, :, None], 0.0), axis=1)
    earlier = (
        jnp.arange(tok_rows, dtype=jnp.int32)[:, None] > jnp.arange(tok_rows, dtype=jnp.int32)[None, :]
    ).astype(jnp.bfloat16)
    rank = jnp.dot(earlier, routed.astype(jnp.bfloat16), preferred_element_type=jnp.float32)
    in_slot = routed.T[:, None, :] & (
        rank.T[:, None, :] == jnp.arange(capacity, dtype=jnp.float32)[None, :, None]
    )
    slot_gate = jnp.where(in_slot, gate_of.T[:, None, :], 0.0).reshape(total, tok_rows)
    pick = in_slot.reshape(total, tok_rows).astype(jnp.bfloat16)
    gate_of_slot = jnp.sum(slot_gate, axis=1)
    layout = (sources, per_device, capacity, model_width)
    send_inputs = jnp.dot(pick, tokens, preferred_element_type=jnp.bfloat16)
    grad_of_slot = jnp.dot(pick, out_grad, preferred_element_type=jnp.float32)
    send_grads = (gate_of_slot[:, None] * grad_of_slot).astype(jnp.bfloat16)

    inputs_here = lax.all_to_all(
        send_inputs.reshape(layout), "expert", split_axis=0, concat_axis=0, tiled=True
    )
    grad_rows = lax.all_to_all(
        send_grads.reshape(layout), "expert", split_axis=0, concat_axis=0, tiled=True
    )
    projected_here, activation_here, results_here = lax.optimization_barrier(
        expert_forward(inputs_here, full_in, full_down)
    )
    results_home = lax.all_to_all(results_here, "expert", split_axis=0, concat_axis=0, tiled=True)
    grad_hidden, grad_inputs = expert_backward(projected_here, grad_rows, full_in, full_down)

    grad_in = (
        jnp.einsum("sxcd,sxcj->xdj", inputs_here, grad_hidden, preferred_element_type=jnp.float32)
        * model_width ** (-0.5)
    ).astype(jnp.bfloat16)
    grad_down = (
        jnp.einsum("sxcf,sxcd->xfd", activation_here, grad_rows, preferred_element_type=jnp.float32)
        * hidden_units ** (-0.5)
    ).astype(jnp.bfloat16)
    packed_g = jnp.concatenate([to_owner_rows(grad_in, owners), to_owner_rows(grad_down, owners)], axis=1)
    packed_g = packed_g.reshape(owners * 8, -1)
    summed = lax.psum_scatter(packed_g, "dp", scatter_dimension=0, tiled=True)
    summed = summed.reshape(1, -1).astype(jnp.float32)
    summed_in = from_owner_rows(summed[:, : per_device * in_size], 1, per_device, in_rows, in_cols)
    summed_down = from_owner_rows(
        summed[:, per_device * in_size :], 1, per_device, down_rows, down_cols
    )

    inputs_back = lax.all_to_all(grad_inputs, "expert", split_axis=0, concat_axis=0, tiled=True)

    new_w_in = (w_in.astype(jnp.float32) - step_rate * summed_in).astype(jnp.bfloat16)
    new_w_down = (w_down.astype(jnp.float32) - step_rate * summed_down).astype(jnp.bfloat16)
    inputs_back, new_w_in, new_w_down = lax.optimization_barrier((inputs_back, new_w_in, new_w_down))

    moe_out = jnp.einsum(
        "st,sd->td",
        slot_gate,
        results_home.reshape(total, model_width).astype(jnp.float32),
        precision=lax.Precision.HIGHEST,
        preferred_element_type=jnp.float32,
    ).astype(jnp.bfloat16)
    token_grad = jnp.einsum(
        "st,sd->td",
        pick,
        inputs_back.reshape(total, model_width),
        preferred_element_type=jnp.float32,
    ).astype(jnp.bfloat16)

    return (moe_out, token_grad, new_w_in, new_w_down)


def solution(mesh):
    return jax.shard_map(
        body,
        mesh=mesh,
        in_specs=(
            P(("dp", "expert"), None),
            P(("dp", "expert"), None),
            P(("dp", "expert"), None),
            P("expert", "dp", None),
            P("expert", "dp", None),
            P(("dp", "expert"), None),
        ),
        out_specs=(
            P(("dp", "expert"), None),
            P(("dp", "expert"), None),
            P("expert", "dp", None),
            P("expert", "dp", None),
        ),
        check_vma=False,
    )
```

```python
import jax
import jax.numpy as jnp
from jax import lax
from jax.experimental import pallas as pl
from jax.experimental.pallas import tpu as pltpu
from jax.sharding import PartitionSpec as P

step_rate = 0.5


def dispatch_kernel(pick_ref, rows_ref, out_ref):
    out_ref[...] = jnp.dot(
        pick_ref[...], rows_ref[...], preferred_element_type=jnp.float32
    ).astype(out_ref.dtype)


def dispatch_rows(pick, rows):
    slots, count = pick.shape
    width = rows.shape[1]
    block = 256
    return pl.pallas_call(
        dispatch_kernel,
        out_shape=jax.ShapeDtypeStruct((slots, width), jnp.bfloat16),
        grid=(slots // block,),
        in_specs=[
            pl.BlockSpec((block, count), lambda i: (i, 0)),
            pl.BlockSpec((count, width), lambda i: (0, 0)),
        ],
        out_specs=pl.BlockSpec((block, width), lambda i: (i, 0)),
        cost_estimate=pl.CostEstimate(
            flops=2 * slots * count * width,
            bytes_accessed=2 * (slots * count + count * width + slots * width),
            transcendentals=0,
        ),
        name="dispatch_rows",
    )(pick, rows)


def expert_forward(inputs, full_in, full_down):
    model_width = full_in.shape[1]
    hidden_units = full_down.shape[1]
    projected = jnp.einsum(
        "sxcd,xdj->sxcj", inputs, full_in, preferred_element_type=jnp.float32
    ) * model_width ** (-0.5)
    gate_part = projected[..., :hidden_units]
    up_part = projected[..., hidden_units:]
    activation = (jax.nn.silu(gate_part) * up_part).astype(jnp.bfloat16)
    results = (
        jnp.einsum("sxcf,xfd->sxcd", activation, full_down, preferred_element_type=jnp.float32)
        * hidden_units ** (-0.5)
    ).astype(jnp.bfloat16)
    return (projected, activation, results)


def expert_backward(projected, grad_rows, full_in, full_down):
    model_width = full_in.shape[1]
    hidden_units = full_down.shape[1]
    grad_act = jnp.einsum(
        "sxcd,xfd->sxcf", grad_rows, full_down, preferred_element_type=jnp.float32
    ) * hidden_units ** (-0.5)
    gate_part = projected[..., :hidden_units]
    up_part = projected[..., hidden_units:]
    sigmoid_gate = jax.nn.sigmoid(gate_part)
    grad_gate = grad_act * up_part * sigmoid_gate * (1.0 + gate_part * (1.0 - sigmoid_gate))
    grad_up = grad_act * jax.nn.silu(gate_part)
    grad_hidden = jnp.concatenate([grad_gate, grad_up], axis=-1).astype(jnp.bfloat16)
    grad_inputs = (
        jnp.einsum("sxcj,xdj->sxcd", grad_hidden, full_in, preferred_element_type=jnp.float32)
        * model_width ** (-0.5)
    ).astype(jnp.bfloat16)
    return (grad_hidden, grad_inputs)


def to_owner_rows(grad, owners):
    per_device, rows, cols = grad.shape
    part = rows // owners
    return (
        grad.reshape(per_device, owners, part, cols)
        .transpose(1, 0, 2, 3)
        .reshape(owners, per_device * part * cols)
    )


def from_owner_rows(flat, owners, per_device, part, cols):
    return (
        flat.reshape(owners, per_device, part, cols)
        .transpose(1, 0, 2, 3)
        .reshape(per_device, owners * part, cols)
    )


def body(tokens, routes, gates, w_in, w_down, out_grad):
    tok_rows, model_width = tokens.shape
    top_count = routes.shape[1]
    per_device, in_rows, in_cols = w_in.shape
    _, down_rows, down_cols = w_down.shape
    hidden_units = in_cols // 2
    sources = lax.axis_size("expert")
    owners = lax.axis_size("dp")
    experts = per_device * sources
    capacity = min(tok_rows, 2 * tok_rows * top_count // experts)
    total = experts * capacity

    in_size = in_rows * in_cols
    packed_w = jnp.concatenate(
        [w_in.reshape(1, per_device * in_size), w_down.reshape(1, per_device * down_rows * down_cols)],
        axis=1,
    )
    gathered = lax.all_gather(packed_w, "dp", axis=0, tiled=True)
    full_in = from_owner_rows(gathered[:, : per_device * in_size], owners, per_device, in_rows, in_cols)
    full_down = from_owner_rows(
        gathered[:, per_device * in_size :], owners, per_device, down_rows, down_cols
    )

    named = routes[:, :, None] == jnp.arange(experts, dtype=jnp.int32)[None, None, :]
    routed = jnp.any(named, axis=1)
    gate_of = jnp.sum(jnp.where(named, gates[:, :, None], 0.0), axis=1)
    earlier = (
        jnp.arange(tok_rows, dtype=jnp.int32)[:, None] > jnp.arange(tok_rows, dtype=jnp.int32)[None, :]
    ).astype(jnp.bfloat16)
    rank = jnp.dot(earlier, routed.astype(jnp.bfloat16), preferred_element_type=jnp.float32)
    in_slot = routed.T[:, None, :] & (
        rank.T[:, None, :] == jnp.arange(capacity, dtype=jnp.float32)[None, :, None]
    )
    slot_gate = jnp.where(in_slot, gate_of.T[:, None, :], 0.0).reshape(total, tok_rows)
    pick = in_slot.reshape(total, tok_rows).astype(jnp.bfloat16)
    gate_of_slot = jnp.sum(slot_gate, axis=1)
    layout = (sources, per_device, capacity, model_width)
    send_inputs = dispatch_rows(pick, tokens)
    grad_of_slot = jnp.dot(pick, out_grad, preferred_element_type=jnp.float32)
    send_grads = (gate_of_slot[:, None] * grad_of_slot).astype(jnp.bfloat16)

    inputs_here = lax.all_to_all(
        send_inputs.reshape(layout), "expert", split_axis=0, concat_axis=0, tiled=True
    )
    grad_rows = lax.all_to_all(
        send_grads.reshape(layout), "expert", split_axis=0, concat_axis=0, tiled=True
    )
    projected_here, activation_here, results_here = lax.optimization_barrier(
        expert_forward(inputs_here, full_in, full_down)
    )
    results_home = lax.all_to_all(results_here, "expert", split_axis=0, concat_axis=0, tiled=True)
    grad_hidden, grad_inputs = expert_backward(projected_here, grad_rows, full_in, full_down)

    grad_in = (
        jnp.einsum("sxcd,sxcj->xdj", inputs_here, grad_hidden, preferred_element_type=jnp.float32)
        * model_width ** (-0.5)
    ).astype(jnp.bfloat16)
    grad_down = (
        jnp.einsum("sxcf,sxcd->xfd", activation_here, grad_rows, preferred_element_type=jnp.float32)
        * hidden_units ** (-0.5)
    ).astype(jnp.bfloat16)
    packed_g = jnp.concatenate([to_owner_rows(grad_in, owners), to_owner_rows(grad_down, owners)], axis=1)
    packed_g = packed_g.reshape(owners * 8, -1)
    summed = lax.psum_scatter(packed_g, "dp", scatter_dimension=0, tiled=True)
    summed = summed.reshape(1, -1).astype(jnp.float32)
    summed_in = from_owner_rows(summed[:, : per_device * in_size], 1, per_device, in_rows, in_cols)
    summed_down = from_owner_rows(
        summed[:, per_device * in_size :], 1, per_device, down_rows, down_cols
    )

    inputs_back = lax.all_to_all(grad_inputs, "expert", split_axis=0, concat_axis=0, tiled=True)

    new_w_in = (w_in.astype(jnp.float32) - step_rate * summed_in).astype(jnp.bfloat16)
    new_w_down = (w_down.astype(jnp.float32) - step_rate * summed_down).astype(jnp.bfloat16)
    inputs_back, new_w_in, new_w_down = lax.optimization_barrier((inputs_back, new_w_in, new_w_down))

    moe_out = jnp.einsum(
        "st,sd->td",
        slot_gate,
        results_home.reshape(total, model_width).astype(jnp.float32),
        precision=lax.Precision.HIGHEST,
        preferred_element_type=jnp.float32,
    ).astype(jnp.bfloat16)
    token_grad = jnp.einsum(
        "st,sd->td",
        pick,
        inputs_back.reshape(total, model_width),
        preferred_element_type=jnp.float32,
    ).astype(jnp.bfloat16)

    return (moe_out, token_grad, new_w_in, new_w_down)


def solution(mesh):
    return jax.shard_map(
        body,
        mesh=mesh,
        in_specs=(
            P(("dp", "expert"), None),
            P(("dp", "expert"), None),
            P(("dp", "expert"), None),
            P("expert", "dp", None),
            P("expert", "dp", None),
            P(("dp", "expert"), None),
        ),
        out_specs=(
            P(("dp", "expert"), None),
            P(("dp", "expert"), None),
            P("expert", "dp", None),
            P("expert", "dp", None),
        ),
        check_vma=False,
    )
```

```python
import jax
import jax.numpy as jnp
from jax import lax
from jax.sharding import PartitionSpec as P

step_rate = 0.5


def expert_forward(inputs, full_in, full_down):
    model_width = full_in.shape[1]
    hidden_units = full_down.shape[1]
    projected = jnp.einsum(
        "sxcd,xdj->sxcj", inputs, full_in, preferred_element_type=jnp.float32
    ) * model_width ** (-0.5)
    gate_part = projected[..., :hidden_units]
    up_part = projected[..., hidden_units:]
    activation = (jax.nn.silu(gate_part) * up_part).astype(jnp.bfloat16)
    results = (
        jnp.einsum("sxcf,xfd->sxcd", activation, full_down, preferred_element_type=jnp.float32)
        * hidden_units ** (-0.5)
    ).astype(jnp.bfloat16)
    return (projected, activation, results)


def expert_backward(projected, grad_rows, full_in, full_down):
    model_width = full_in.shape[1]
    hidden_units = full_down.shape[1]
    grad_act = jnp.einsum(
        "sxcd,xfd->sxcf", grad_rows, full_down, preferred_element_type=jnp.float32
    ) * hidden_units ** (-0.5)
    gate_part = projected[..., :hidden_units]
    up_part = projected[..., hidden_units:]
    sigmoid_gate = jax.nn.sigmoid(gate_part)
    grad_gate = grad_act * up_part * sigmoid_gate * (1.0 + gate_part * (1.0 - sigmoid_gate))
    grad_up = grad_act * jax.nn.silu(gate_part)
    grad_hidden = jnp.concatenate([grad_gate, grad_up], axis=-1).astype(jnp.bfloat16)
    grad_inputs = (
        jnp.einsum("sxcj,xdj->sxcd", grad_hidden, full_in, preferred_element_type=jnp.float32)
        * model_width ** (-0.5)
    ).astype(jnp.bfloat16)
    return (grad_hidden, grad_inputs)


def to_owner_rows(grad, owners):
    per_device, rows, cols = grad.shape
    part = rows // owners
    return (
        grad.reshape(per_device, owners, part, cols)
        .transpose(1, 0, 2, 3)
        .reshape(owners, per_device * part * cols)
    )


def from_owner_rows(flat, owners, per_device, part, cols):
    return (
        flat.reshape(owners, per_device, part, cols)
        .transpose(1, 0, 2, 3)
        .reshape(per_device, owners * part, cols)
    )


def body(tokens, routes, gates, w_in, w_down, out_grad):
    tok_rows, model_width = tokens.shape
    top_count = routes.shape[1]
    per_device, in_rows, in_cols = w_in.shape
    _, down_rows, down_cols = w_down.shape
    hidden_units = in_cols // 2
    sources = lax.axis_size("expert")
    owners = lax.axis_size("dp")
    experts = per_device * sources
    capacity = min(tok_rows, 2 * tok_rows * top_count // experts)
    total = experts * capacity

    in_size = in_rows * in_cols
    packed_w = jnp.concatenate(
        [w_in.reshape(1, per_device * in_size), w_down.reshape(1, per_device * down_rows * down_cols)],
        axis=1,
    )
    gathered = lax.all_gather(packed_w, "dp", axis=0, tiled=True)
    full_in = from_owner_rows(gathered[:, : per_device * in_size], owners, per_device, in_rows, in_cols)
    full_down = from_owner_rows(
        gathered[:, per_device * in_size :], owners, per_device, down_rows, down_cols
    )

    named = routes.T[None, :, :] == jnp.arange(experts, dtype=jnp.int32)[:, None, None]
    routed = jnp.any(named, axis=1)
    gate_of = jnp.sum(jnp.where(named, gates.T[None, :, :], 0.0), axis=1)
    later = (
        jnp.arange(tok_rows, dtype=jnp.int32)[:, None] < jnp.arange(tok_rows, dtype=jnp.int32)[None, :]
    ).astype(jnp.bfloat16)
    rank = jnp.dot(routed.astype(jnp.bfloat16), later, preferred_element_type=jnp.float32)
    in_slot = routed[:, None, :] & (
        rank[:, None, :] == jnp.arange(capacity, dtype=jnp.float32)[None, :, None]
    )
    slot_gate = jnp.where(in_slot, gate_of[:, None, :], 0.0).reshape(total, tok_rows)
    pick = in_slot.reshape(total, tok_rows).astype(jnp.bfloat16)
    gate_of_slot = jnp.sum(slot_gate, axis=1)
    layout = (sources, per_device, capacity, model_width)
    send_inputs = jnp.dot(pick, tokens, preferred_element_type=jnp.bfloat16)
    grad_of_slot = jnp.dot(pick, out_grad, preferred_element_type=jnp.float32)
    send_grads = (gate_of_slot[:, None] * grad_of_slot).astype(jnp.bfloat16)

    inputs_here = lax.all_to_all(
        send_inputs.reshape(layout), "expert", split_axis=0, concat_axis=0, tiled=True
    )
    grad_rows = lax.all_to_all(
        send_grads.reshape(layout), "expert", split_axis=0, concat_axis=0, tiled=True
    )
    projected_here, activation_here, results_here = lax.optimization_barrier(
        expert_forward(inputs_here, full_in, full_down)
    )
    results_home = lax.all_to_all(results_here, "expert", split_axis=0, concat_axis=0, tiled=True)
    grad_hidden, grad_inputs = expert_backward(projected_here, grad_rows, full_in, full_down)

    grad_in = (
        jnp.einsum("sxcd,sxcj->xdj", inputs_here, grad_hidden, preferred_element_type=jnp.float32)
        * model_width ** (-0.5)
    ).astype(jnp.bfloat16)
    grad_down = (
        jnp.einsum("sxcf,sxcd->xfd", activation_here, grad_rows, preferred_element_type=jnp.float32)
        * hidden_units ** (-0.5)
    ).astype(jnp.bfloat16)
    packed_g = jnp.concatenate([to_owner_rows(grad_in, owners), to_owner_rows(grad_down, owners)], axis=1)
    packed_g = packed_g.reshape(owners * 8, -1)
    summed = lax.psum_scatter(packed_g, "dp", scatter_dimension=0, tiled=True)
    summed = summed.reshape(1, -1).astype(jnp.float32)
    summed_in = from_owner_rows(summed[:, : per_device * in_size], 1, per_device, in_rows, in_cols)
    summed_down = from_owner_rows(
        summed[:, per_device * in_size :], 1, per_device, down_rows, down_cols
    )

    inputs_back = lax.all_to_all(grad_inputs, "expert", split_axis=0, concat_axis=0, tiled=True)

    new_w_in = (w_in.astype(jnp.float32) - step_rate * summed_in).astype(jnp.bfloat16)
    new_w_down = (w_down.astype(jnp.float32) - step_rate * summed_down).astype(jnp.bfloat16)
    inputs_back, new_w_in, new_w_down = lax.optimization_barrier((inputs_back, new_w_in, new_w_down))

    moe_out = jnp.einsum(
        "st,sd->td",
        slot_gate,
        results_home.reshape(total, model_width).astype(jnp.float32),
        precision=lax.Precision.HIGHEST,
        preferred_element_type=jnp.float32,
    ).astype(jnp.bfloat16)
    token_grad = jnp.einsum(
        "st,sd->td",
        pick,
        inputs_back.reshape(total, model_width),
        preferred_element_type=jnp.float32,
    ).astype(jnp.bfloat16)

    return (moe_out, token_grad, new_w_in, new_w_down)


def solution(mesh):
    return jax.shard_map(
        body,
        mesh=mesh,
        in_specs=(
            P(("dp", "expert"), None),
            P(("dp", "expert"), None),
            P(("dp", "expert"), None),
            P("expert", "dp", None),
            P("expert", "dp", None),
            P(("dp", "expert"), None),
        ),
        out_specs=(
            P(("dp", "expert"), None),
            P(("dp", "expert"), None),
            P("expert", "dp", None),
            P("expert", "dp", None),
        ),
        check_vma=False,
    )
```
